512 devices in a mesh: seq: 128 (over z, x, core), fsdp: 4 (over y).
Axes of the slice: x: 4, y: 4, z: 16, core: 2. Of those that a mesh axis runs over, the one named last changes fastest.
Arguments:
- query_key: bfloat16 [131072, 3072], P(('seq', 'fsdp')), may hold values from -48 to 48
- values: bfloat16 [131072, 3072], P(('seq', 'fsdp')), may hold values from -6 to 6
- cluster_ids: int32 [24, 1024], replicated, may hold values from 0 to 127, as said below
Outputs:
- attended: bfloat16 [131072, 3072], P(('seq', 'fsdp'))
The draws below stay inside these ranges and needn't reach their ends.
Inputs may be any that keep to these rules, and one draw needn't show every extreme that they name: `cluster_ids`: for every head and cluster at most 10 blocks name that cluster, and for every head some cluster is named by exactly 10 blocks. Among the (head, block) pairs of one group of 6 consecutive heads and one run of 8 blocks starting at a multiple of 8, no cluster is named more than 1 times, and some cluster exactly 1 times; the blocks of one such run name distinct clusters for each head.
All inputs are finite; a program needn't handle non-finite values.
Results may differ from the reference program's by a relative error of at most 0.0027.
Values may be sent and summed in bfloat16 or wider, within the bound.
No kernel may reach another device: no remote copies, remote signals or barrier semaphores. Data moves between devices by JAX's collectives and lax.ppermute only.
A program may use at most 64 MiB of HBM per device.

```python
import math
import jax
import jax.numpy as jnp
from jax import lax

HEADS = 24
HD = 128
BLK = 128
HPG = 6
B_SHARD = 8
CLUSTERS = 128
NBLK = 1024
SEQLEN = 131072
HOT = 2
CAPB = 10


def draw_cluster_ids(key, part):

    def one_group(group_key):
        key_start, key_base, key_label, key_order = jax.random.split(group_key, 4)
        hot_start = jax.random.randint(key_start, (), 0, CLUSTERS)
        position_ids = jnp.arange(CLUSTERS, dtype=jnp.int32)
        relative = (position_ids - hot_start) % CLUSTERS
        multiplicity = 1 + (relative < HOT).astype(jnp.int32) - ((relative >= B_SHARD) & (relative < B_SHARD + HOT)).astype(jnp.int32)
        running = jnp.cumsum(multiplicity)
        shard_ids = jnp.arange(CLUSTERS, dtype=jnp.int32)
        sorted_start = jnp.sum((running[None, :] <= shard_ids[:, None]).astype(jnp.int32), axis=1)
        base_offset = jax.random.permutation(key_base, sorted_start)
        relabel = jax.random.permutation(key_label, CLUSTERS)
        block_order = jax.vmap(lambda order_key: jax.random.permutation(order_key, B_SHARD))(jax.random.split(key_order, CLUSTERS))
        offsets = B_SHARD * jnp.arange(HPG, dtype=jnp.int32)[:, None, None] + block_order[None, :, :]
        virtual = (base_offset[None, :, None] + offsets) % CLUSTERS
        return relabel[virtual].reshape(HPG, CLUSTERS * B_SHARD)
    group_keys = jax.random.split(jax.random.fold_in(key, 7), HEADS // HPG)
    return jax.vmap(one_group)(group_keys).reshape(HEADS, NBLK).astype(jnp.int32)


def draw_query_key(key, part):
    key_main = jax.random.fold_in(jax.random.fold_in(key, 11), 0)
    full_shape = (SEQLEN // 2, 2, HEADS * HD)
    entries = jax.random.normal(key_main, full_shape, jnp.float32) * 0.6
    return jnp.clip(entries, -48.0, 48.0).reshape(SEQLEN, HEADS * HD).astype(jnp.bfloat16)


def shard_levels(key, dims, cuts, least, largest):
    factor_of = 1.0
    for axis_at, shards_of in cuts:
        steps = jax.random.uniform(jax.random.fold_in(jax.random.fold_in(key, 6), axis_at), (shards_of,), jnp.float32, least / len(cuts), largest / len(cuts))
        factor_of = factor_of * jnp.repeat(jnp.exp(steps), dims[axis_at] // shards_of).reshape((-1,) + (1,) * (len(dims) - 1 - axis_at))
    return factor_of


def centred(rng, shape, spread, bound, cuts=(), held_as=jnp.bfloat16):
    factor_of = shard_levels(rng, shape, cuts, -0.22, 0.18) if cuts else 1.0
    values = jax.random.normal(rng, shape, jnp.float32) * spread * factor_of
    return jnp.minimum(jnp.maximum(values, -bound), bound).astype(held_as)


def setup_inputs(seed: int = 0) -> dict:
    arg_keys = jax.random.split(jax.random.key(seed), 4)
    return {
        "query_key": draw_query_key(jax.random.fold_in(arg_keys[3], 71), 0),
        "values": centred(arg_keys[1], (SEQLEN, HEADS * HD), 1.0, 6.0, ((0, 512),)),
        "cluster_ids": draw_cluster_ids(jax.random.fold_in(arg_keys[3], 71), 0),
    }


masked_score = -1e+30

def cluster_attention(query_rows, value_rows, positions, alive_rows):
    scores = jnp.dot(query_rows, query_rows.T, preferred_element_type=jnp.float32) * (1.0 / math.sqrt(HD))
    allowed = alive_rows[None, :] & (positions[None, :] <= positions[:, None])
    scores = jnp.where(allowed, scores, masked_score)
    row_peak = lax.optimization_barrier(jnp.max(scores, axis=1, keepdims=True))
    weights = jnp.where(allowed, jnp.exp(scores - row_peak), 0.0)
    row_total = jnp.where(alive_rows[:, None], lax.optimization_barrier(jnp.sum(weights, axis=1, keepdims=True)), 1.0)
    weighted = jnp.dot(weights.astype(jnp.bfloat16), value_rows, preferred_element_type=jnp.float32)
    return (weighted / row_total).astype(jnp.bfloat16)

def reference(query_key, values, cluster_ids):
    block_ids = jnp.arange(NBLK, dtype=jnp.int32)
    offsets = jnp.arange(BLK, dtype=jnp.int32)
    cluster_range = jnp.arange(CLUSTERS, dtype=jnp.int32)

    def one_head(head_index):
        labels = lax.dynamic_index_in_dim(cluster_ids, head_index, 0, keepdims=False)
        onehot = (labels[:, None] == cluster_range[None, :]).astype(jnp.int32)
        ordinal = lax.optimization_barrier(jnp.sum((jnp.cumsum(onehot, axis=0) - onehot) * onehot, axis=1))
        members = jnp.full((CLUSTERS, CAPB), NBLK, jnp.int32).at[labels, ordinal].set(block_ids)
        head_keys = lax.dynamic_slice_in_dim(query_key, head_index * HD, HD, 1).reshape(NBLK, BLK, HD)
        head_values = lax.dynamic_slice_in_dim(values, head_index * HD, HD, 1).reshape(NBLK, BLK, HD)
        zero_block = jnp.zeros((1, BLK, HD), query_key.dtype)
        key_table = jnp.concatenate([head_keys, zero_block], axis=0)
        value_table = jnp.concatenate([head_values, zero_block], axis=0)

        def one_cluster(member_row):
            alive_blocks = member_row < NBLK
            query_rows = key_table[member_row].reshape(CAPB * BLK, HD)
            value_rows = value_table[member_row].reshape(CAPB * BLK, HD)
            positions = (member_row[:, None] * BLK + offsets[None, :]).reshape(CAPB * BLK)
            alive_rows = jnp.repeat(alive_blocks, BLK)
            return cluster_attention(query_rows, value_rows, positions, alive_rows)
        results = lax.map(one_cluster, members)
        placed = jnp.zeros((NBLK + 1, BLK, HD), jnp.bfloat16)
        placed = placed.at[members.reshape(CLUSTERS * CAPB)].set(results.reshape(CLUSTERS * CAPB, BLK, HD))
        return placed[:NBLK].reshape(SEQLEN, HD)
    heads_out = lax.map(one_head, jnp.arange(HEADS, dtype=jnp.int32))
    return jnp.transpose(heads_out, (1, 0, 2)).reshape(SEQLEN, HEADS * HD)
```

```python
import math

import jax
import jax.numpy as jnp
from jax import lax
from jax.sharding import PartitionSpec as P

BLK = 128


masked_score = -1e30


def by_index(source_table, row_index):
    padded = jnp.concatenate(
        [source_table, jnp.zeros((1,) + source_table.shape[1:], source_table.dtype)], axis=0
    )
    return padded[row_index]


def softmax_group(key_rows, positions, alive_rows, score_scale):
    half = BLK // 2
    blocks = key_rows.shape[0] // BLK

    def by_half(rows):
        shaped = rows.reshape((blocks, 2, half) + rows.shape[1:])
        return jnp.swapaxes(shaped, 0, 1).reshape(rows.shape)

    query_rows = by_half(key_rows)
    query_positions = by_half(positions)
    query_alive = by_half(alive_rows)
    scores = jnp.dot(query_rows, key_rows.T, preferred_element_type=jnp.float32) * score_scale
    allowed = alive_rows[None, :] & (positions[None, :] <= query_positions[:, None])
    scores = jnp.where(allowed, scores, masked_score)
    row_peak = jnp.max(scores, axis=1, keepdims=True)
    weights = jnp.where(allowed, jnp.exp(scores - row_peak), 0.0)
    row_total = jnp.where(query_alive[:, None], jnp.sum(weights, axis=1, keepdims=True), 1.0)
    weights = weights.astype(jnp.bfloat16).reshape(2, blocks * half, key_rows.shape[0])
    row_total = row_total.reshape(2, blocks * half, 1)
    return weights[0], weights[1], row_total[0], row_total[1]


def shards(query_key, values, cluster_ids):
    seq_count = lax.axis_size("seq")
    group_count = lax.axis_size("fsdp")
    seq_index = lax.axis_index("seq")
    group_index = lax.axis_index("fsdp")
    heads_all = cluster_ids.shape[0]
    group_heads = heads_all // group_count
    head_dim = query_key.shape[1] // heads_all
    tok_rows = query_key.shape[0]
    shard_blocks = group_count * tok_rows // BLK
    all_blocks = cluster_ids.shape[1]
    item_count = group_heads * shard_blocks
    slot_count = max(1, item_count // seq_count)
    capacity = shard_blocks + min(shard_blocks // 4, seq_count - shard_blocks)
    group_rows = capacity * BLK
    send_rows = seq_count * slot_count
    score_scale = 1.0 / math.sqrt(head_dim)
    keys_local, values_local = (
        lax.all_to_all(query_key, "fsdp", split_axis=1, concat_axis=0, tiled=True),
        lax.all_to_all(values, "fsdp", split_axis=1, concat_axis=0, tiled=True),
    )

    def into_items(block_data):
        shaped = block_data.reshape(shard_blocks, BLK, group_heads, head_dim)
        return jnp.transpose(shaped, (2, 0, 1, 3)).reshape(item_count, BLK, head_dim)

    key_items = into_items(keys_local)
    value_items = into_items(values_local)
    group_ids = lax.dynamic_slice_in_dim(cluster_ids, group_index * group_heads, group_heads, 0)
    by_source = jnp.transpose(
        group_ids.reshape(group_heads, seq_count, shard_blocks), (1, 0, 2)
    ).reshape(seq_count, item_count)
    own_dest = lax.dynamic_index_in_dim(by_source, seq_index, 0, keepdims=False)
    item_ids = jnp.arange(item_count, dtype=jnp.int32)
    earlier = (own_dest[None, :] == own_dest[:, None]) & (item_ids[None, :] < item_ids[:, None])
    own_pos = own_dest * slot_count + jnp.sum(earlier.astype(jnp.int32), axis=1)
    row_ids = jnp.arange(send_rows, dtype=jnp.int32)
    slot_match = own_pos[None, :] == row_ids[:, None]
    send_pick = jnp.sum(jnp.where(slot_match, item_ids[None, :], 0), axis=1) + item_count * (
        1 - jnp.any(slot_match, axis=1).astype(jnp.int32)
    )
    received_mask = (by_source == seq_index).astype(jnp.int32)
    recv_pos = (
        jnp.arange(seq_count, dtype=jnp.int32)[:, None] * slot_count
        + jnp.cumsum(received_mask, axis=1)
        - received_mask
    )
    recv_by_head = jnp.transpose(
        recv_pos.reshape(seq_count, group_heads, shard_blocks), (1, 0, 2)
    ).reshape(group_heads * all_blocks)
    owned_mask = (group_ids == seq_index).astype(jnp.int32)
    ordinal = jnp.cumsum(owned_mask, axis=1) - owned_mask
    target = jnp.where(
        owned_mask > 0, jnp.arange(group_heads, dtype=jnp.int32)[:, None] * capacity + ordinal, -1
    ).reshape(group_heads * all_blocks)
    slot_ids = jnp.arange(group_heads * capacity, dtype=jnp.int32)
    matches = target[None, :] == slot_ids[:, None]
    present = jnp.any(matches, axis=1)
    source_row = jnp.sum(jnp.where(matches, recv_by_head[None, :], 0), axis=1) + send_rows * (
        1 - present.astype(jnp.int32)
    )
    block_ids = jnp.tile(jnp.arange(all_blocks, dtype=jnp.int32), group_heads)
    block_of = jnp.sum(jnp.where(matches, block_ids[None, :], 0), axis=1)
    arrived_k = lax.all_to_all(
        by_index(key_items, send_pick), "seq", split_axis=0, concat_axis=0, tiled=True
    )
    arrived_v = lax.all_to_all(
        by_index(value_items, send_pick), "seq", split_axis=0, concat_axis=0, tiled=True
    )
    key_grouped = by_index(arrived_k, source_row)
    value_grouped = by_index(arrived_v, source_row)
    positions = (block_of[:, None] * BLK + jnp.arange(BLK, dtype=jnp.int32)[None, :]).reshape(
        group_heads, group_rows
    )
    alive_rows = jnp.repeat(present, BLK).reshape(group_heads, group_rows)

    def one_head(operands):
        key_rows, where_at, alive_here = operands
        return softmax_group(key_rows, where_at, alive_here, score_scale)

    weights_0, weights_1, totals_0, totals_1 = lax.map(
        one_head,
        (key_grouped.reshape(group_heads, group_rows, head_dim), positions, alive_rows),
    )
    half = BLK // 2
    value_rows = value_grouped.reshape(group_heads, group_rows, head_dim)
    back_match = source_row[None, :] == row_ids[:, None]
    back_pick = jnp.sum(
        jnp.where(back_match, slot_ids[None, :], 0), axis=1
    ) + group_heads * capacity * (1 - jnp.any(back_match, axis=1).astype(jnp.int32))
    pieces = []
    for part in range(2):
        part_weights = (weights_0, weights_1)[part]
        weighted = jnp.einsum(
            "hqk,hkd->hqd", part_weights, value_rows, preferred_element_type=jnp.float32
        )
        part_total = (totals_0, totals_1)[part]
        outputs = (weighted / part_total).astype(jnp.bfloat16)
        outputs = outputs.reshape(group_heads * capacity, half, head_dim)
        returned = lax.all_to_all(
            by_index(outputs, back_pick), "seq", split_axis=0, concat_axis=0, tiled=True
        )
        own_output = by_index(returned, own_pos)
        token_major = jnp.transpose(
            own_output.reshape(group_heads, shard_blocks, half, head_dim), (1, 2, 0, 3)
        ).reshape(shard_blocks * half, group_heads * head_dim)
        pieces.append(
            lax.all_to_all(token_major, "fsdp", split_axis=0, concat_axis=1, tiled=True)
        )
    own_blocks = tok_rows // BLK
    joined = jnp.stack(
        [piece.reshape(own_blocks, half, heads_all * head_dim) for piece in pieces], axis=1
    )
    return joined.reshape(tok_rows, heads_all * head_dim)


def solution(mesh):
    placed = (P(("seq", "fsdp"), None), P(("seq", "fsdp"), None), P())
    return jax.shard_map(
        shards, mesh=mesh, in_specs=placed, out_specs=P(("seq", "fsdp"), None), check_vma=False
    )
```

```python
import math

import jax
import jax.numpy as jnp
from jax import lax
from jax.sharding import PartitionSpec as P

BLK = 128


masked_score = -1e30


def by_index(source_table, row_index):
    padded = jnp.concatenate(
        [source_table, jnp.zeros((1,) + source_table.shape[1:], source_table.dtype)], axis=0
    )
    return padded[row_index]


def softmax_group(key_rows, positions, alive_rows, score_scale):
    half = BLK // 2
    blocks = key_rows.shape[0] // BLK

    def by_half(rows):
        shaped = rows.reshape((blocks, 2, half) + rows.shape[1:])
        return jnp.swapaxes(shaped, 0, 1).reshape(rows.shape)

    query_rows = by_half(key_rows)
    query_positions = by_half(positions)
    query_alive = by_half(alive_rows)
    scores = jnp.dot(query_rows, key_rows.T, preferred_element_type=jnp.float32) * score_scale
    allowed = alive_rows[None, :] & (positions[None, :] <= query_positions[:, None])
    scores = jnp.where(allowed, scores, masked_score)
    row_peak = jnp.max(scores, axis=1, keepdims=True)
    weights = jnp.where(allowed, jnp.exp(scores - row_peak), 0.0)
    row_total = jnp.where(query_alive[:, None], jnp.sum(weights, axis=1, keepdims=True), 1.0)
    weights = weights.astype(jnp.bfloat16).reshape(2, blocks * half, key_rows.shape[0])
    row_total = row_total.reshape(2, blocks * half, 1)
    return weights[0], weights[1], row_total[0], row_total[1]


def shards(query_key, values, cluster_ids):
    seq_count = lax.axis_size("seq")
    group_count = lax.axis_size("fsdp")
    seq_index = lax.axis_index("seq")
    group_index = lax.axis_index("fsdp")
    heads_all = cluster_ids.shape[0]
    group_heads = heads_all // group_count
    head_dim = query_key.shape[1] // heads_all
    tok_rows = query_key.shape[0]
    shard_blocks = group_count * tok_rows // BLK
    all_blocks = cluster_ids.shape[1]
    item_count = group_heads * shard_blocks
    slot_count = max(1, item_count // seq_count)
    capacity = shard_blocks + min(shard_blocks // 4, seq_count - shard_blocks)
    group_rows = capacity * BLK
    send_rows = seq_count * slot_count
    score_scale = 1.0 / math.sqrt(head_dim)
    own_blocks = tok_rows // BLK

    def item_major(block_data):
        shaped = block_data.reshape(own_blocks, BLK, group_count, group_heads, head_dim)
        return jnp.transpose(shaped, (2, 3, 0, 1, 4))

    both = jnp.stack([item_major(query_key), item_major(values)], axis=1)
    both = lax.all_to_all(both, "fsdp", split_axis=0, concat_axis=3, tiled=True)
    key_items = both[0, 0].reshape(item_count, BLK, head_dim)
    value_items = both[0, 1].reshape(item_count, BLK, head_dim)
    group_ids = lax.dynamic_slice_in_dim(cluster_ids, group_index * group_heads, group_heads, 0)
    by_source = jnp.transpose(
        group_ids.reshape(group_heads, seq_count, shard_blocks), (1, 0, 2)
    ).reshape(seq_count, item_count)
    own_dest = lax.dynamic_index_in_dim(by_source, seq_index, 0, keepdims=False)
    item_ids = jnp.arange(item_count, dtype=jnp.int32)
    earlier = (own_dest[None, :] == own_dest[:, None]) & (item_ids[None, :] < item_ids[:, None])
    own_pos = own_dest * slot_count + jnp.sum(earlier.astype(jnp.int32), axis=1)
    row_ids = jnp.arange(send_rows, dtype=jnp.int32)
    slot_match = own_pos[None, :] == row_ids[:, None]
    send_pick = jnp.sum(jnp.where(slot_match, item_ids[None, :], 0), axis=1) + item_count * (
        1 - jnp.any(slot_match, axis=1).astype(jnp.int32)
    )
    received_mask = (by_source == seq_index).astype(jnp.int32)
    recv_pos = (
        jnp.arange(seq_count, dtype=jnp.int32)[:, None] * slot_count
        + jnp.cumsum(received_mask, axis=1)
        - received_mask
    )
    recv_by_head = jnp.transpose(
        recv_pos.reshape(seq_count, group_heads, shard_blocks), (1, 0, 2)
    ).reshape(group_heads * all_blocks)
    owned_mask = (group_ids == seq_index).astype(jnp.int32)
    ordinal = jnp.cumsum(owned_mask, axis=1) - owned_mask
    target = jnp.where(
        owned_mask > 0, jnp.arange(group_heads, dtype=jnp.int32)[:, None] * capacity + ordinal, -1
    ).reshape(group_heads * all_blocks)
    slot_ids = jnp.arange(group_heads * capacity, dtype=jnp.int32)
    matches = target[None, :] == slot_ids[:, None]
    present = jnp.any(matches, axis=1)
    source_row = jnp.sum(jnp.where(matches, recv_by_head[None, :], 0), axis=1) + send_rows * (
        1 - present.astype(jnp.int32)
    )
    block_ids = jnp.tile(jnp.arange(all_blocks, dtype=jnp.int32), group_heads)
    block_of = jnp.sum(jnp.where(matches, block_ids[None, :], 0), axis=1)
    arrived_k = lax.all_to_all(
        by_index(key_items, send_pick), "seq", split_axis=0, concat_axis=0, tiled=True
    )
    arrived_v = lax.all_to_all(
        by_index(value_items, send_pick), "seq", split_axis=0, concat_axis=0, tiled=True
    )
    key_grouped = by_index(arrived_k, source_row)
    value_grouped = by_index(arrived_v, source_row)
    positions = (block_of[:, None] * BLK + jnp.arange(BLK, dtype=jnp.int32)[None, :]).reshape(
        group_heads, group_rows
    )
    alive_rows = jnp.repeat(present, BLK).reshape(group_heads, group_rows)

    def one_head(operands):
        key_rows, where_at, alive_here = operands
        return softmax_group(key_rows, where_at, alive_here, score_scale)

    weights_0, weights_1, totals_0, totals_1 = lax.map(
        one_head,
        (key_grouped.reshape(group_heads, group_rows, head_dim), positions, alive_rows),
    )
    value_rows = value_grouped.reshape(group_heads, group_rows, head_dim)
    back_match = source_row[None, :] == row_ids[:, None]
    back_pick = jnp.sum(
        jnp.where(back_match, slot_ids[None, :], 0), axis=1
    ) + group_heads * capacity * (1 - jnp.any(back_match, axis=1).astype(jnp.int32))
    halves = []
    for part_weights, part_total in ((weights_0, totals_0), (weights_1, totals_1)):
        weighted = jnp.einsum(
            "hqk,hkd->hqd", part_weights, value_rows, preferred_element_type=jnp.float32
        )
        outputs = (weighted / part_total).astype(jnp.bfloat16)
        halves.append(outputs.reshape(group_heads * capacity, BLK // 2, head_dim))
    outputs = jnp.concatenate(halves, axis=1)
    returned = lax.all_to_all(
        by_index(outputs, back_pick), "seq", split_axis=0, concat_axis=0, tiled=True
    )
    own_output = by_index(returned, own_pos).reshape(
        group_heads, group_count, own_blocks, BLK, head_dim
    )
    gathered = lax.all_to_all(own_output, "fsdp", split_axis=1, concat_axis=0, tiled=True)
    token_major = jnp.transpose(gathered[:, 0], (1, 2, 0, 3))
    return token_major.reshape(tok_rows, heads_all * head_dim)


def solution(mesh):
    placed = (P(("seq", "fsdp"), None), P(("seq", "fsdp"), None), P())
    return jax.shard_map(
        shards, mesh=mesh, in_specs=placed, out_specs=P(("seq", "fsdp"), None), check_vma=False
    )
```

```python
import math

import jax
import jax.numpy as jnp
from jax import lax
from jax.sharding import PartitionSpec as P

BLK = 128


masked_score = -1e30


def by_index(source_table, row_index):
    return source_table[jnp.clip(row_index, 0, source_table.shape[0] - 1)]


def softmax_group(key_rows, positions, alive_rows, score_scale):
    half = BLK // 2
    blocks = key_rows.shape[0] // BLK

    def by_half(rows):
        shaped = rows.reshape((blocks, 2, half) + rows.shape[1:])
        return jnp.swapaxes(shaped, 0, 1).reshape(rows.shape)

    query_rows = by_half(key_rows)
    query_positions = by_half(positions)
    query_alive = by_half(alive_rows)
    scores = jnp.dot(query_rows, key_rows.T, preferred_element_type=jnp.float32) * score_scale
    allowed = alive_rows[None, :] & (positions[None, :] <= query_positions[:, None])
    scores = jnp.where(allowed, scores, masked_score)
    row_peak = jnp.max(scores, axis=1, keepdims=True)
    weights = jnp.where(allowed, jnp.exp(scores - row_peak), 0.0)
    row_total = jnp.where(query_alive[:, None], jnp.sum(weights, axis=1, keepdims=True), 1.0)
    weights = weights.astype(jnp.bfloat16).reshape(2, blocks * half, key_rows.shape[0])
    row_total = row_total.reshape(2, blocks * half, 1)
    return weights[0], weights[1], row_total[0], row_total[1]


def shards(query_key, values, cluster_ids):
    seq_count = lax.axis_size("seq")
    group_count = lax.axis_size("fsdp")
    seq_index = lax.axis_index("seq")
    group_index = lax.axis_index("fsdp")
    heads_all = cluster_ids.shape[0]
    group_heads = heads_all // group_count
    head_dim = query_key.shape[1] // heads_all
    tok_rows = query_key.shape[0]
    shard_blocks = group_count * tok_rows // BLK
    all_blocks = cluster_ids.shape[1]
    item_count = group_heads * shard_blocks
    slot_count = max(1, item_count // seq_count)
    capacity = shard_blocks + min(shard_blocks // 4, seq_count - shard_blocks)
    group_rows = capacity * BLK
    send_rows = seq_count * slot_count
    score_scale = 1.0 / math.sqrt(head_dim)
    own_blocks = tok_rows // BLK

    keys_local, values_local = (
        lax.all_to_all(query_key, "fsdp", split_axis=1, concat_axis=0, tiled=True),
        lax.all_to_all(values, "fsdp", split_axis=1, concat_axis=0, tiled=True),
    )

    def into_items(block_data):
        shaped = block_data.reshape(shard_blocks, BLK, group_heads, head_dim)
        return jnp.transpose(shaped, (2, 0, 1, 3)).reshape(item_count, BLK, head_dim)

    key_items = into_items(keys_local)
    value_items = into_items(values_local)
    group_ids = lax.dynamic_slice_in_dim(cluster_ids, group_index * group_heads, group_heads, 0)
    by_source = jnp.transpose(
        group_ids.reshape(group_heads, seq_count, shard_blocks), (1, 0, 2)
    ).reshape(seq_count, item_count)
    own_dest = lax.dynamic_index_in_dim(by_source, seq_index, 0, keepdims=False)
    item_ids = jnp.arange(item_count, dtype=jnp.int32)
    earlier = (own_dest[None, :] == own_dest[:, None]) & (item_ids[None, :] < item_ids[:, None])
    own_pos = own_dest * slot_count + jnp.sum(earlier.astype(jnp.int32), axis=1)
    row_ids = jnp.arange(send_rows, dtype=jnp.int32)
    slot_match = own_pos[None, :] == row_ids[:, None]
    send_pick = jnp.sum(jnp.where(slot_match, item_ids[None, :], 0), axis=1) + item_count * (
        1 - jnp.any(slot_match, axis=1).astype(jnp.int32)
    )
    received_mask = (by_source == seq_index).astype(jnp.int32)
    recv_pos = (
        jnp.arange(seq_count, dtype=jnp.int32)[:, None] * slot_count
        + jnp.cumsum(received_mask, axis=1)
        - received_mask
    )
    recv_by_head = jnp.transpose(
        recv_pos.reshape(seq_count, group_heads, shard_blocks), (1, 0, 2)
    ).reshape(group_heads * all_blocks)
    owned_mask = (group_ids == seq_index).astype(jnp.int32)
    ordinal = jnp.cumsum(owned_mask, axis=1) - owned_mask
    target = jnp.where(
        owned_mask > 0, jnp.arange(group_heads, dtype=jnp.int32)[:, None] * capacity + ordinal, -1
    ).reshape(group_heads * all_blocks)
    slot_ids = jnp.arange(group_heads * capacity, dtype=jnp.int32)
    matches = target[None, :] == slot_ids[:, None]
    present = jnp.any(matches, axis=1)
    source_row = jnp.sum(jnp.where(matches, recv_by_head[None, :], 0), axis=1) + send_rows * (
        1 - present.astype(jnp.int32)
    )
    block_ids = jnp.tile(jnp.arange(all_blocks, dtype=jnp.int32), group_heads)
    block_of = jnp.sum(jnp.where(matches, block_ids[None, :], 0), axis=1)
    arrived_k = lax.all_to_all(
        by_index(key_items, send_pick), "seq", split_axis=0, concat_axis=0, tiled=True
    )
    arrived_v = lax.all_to_all(
        by_index(value_items, send_pick), "seq", split_axis=0, concat_axis=0, tiled=True
    )
    key_grouped = by_index(arrived_k, source_row)
    value_grouped = by_index(arrived_v, source_row)
    positions = (block_of[:, None] * BLK + jnp.arange(BLK, dtype=jnp.int32)[None, :]).reshape(
        group_heads, group_rows
    )
    alive_rows = jnp.repeat(present, BLK).reshape(group_heads, group_rows)

    def one_head(operands):
        key_rows, where_at, alive_here = operands
        return softmax_group(key_rows, where_at, alive_here, score_scale)

    weights_0, weights_1, totals_0, totals_1 = lax.map(
        one_head,
        (key_grouped.reshape(group_heads, group_rows, head_dim), positions, alive_rows),
    )
    value_rows = value_grouped.reshape(group_heads, group_rows, head_dim)
    back_match = source_row[None, :] == row_ids[:, None]
    back_pick = jnp.sum(
        jnp.where(back_match, slot_ids[None, :], 0), axis=1
    ) + group_heads * capacity * (1 - jnp.any(back_match, axis=1).astype(jnp.int32))
    halves = []
    for part_weights, part_total in ((weights_0, totals_0), (weights_1, totals_1)):
        weighted = jnp.einsum(
            "hqk,hkd->hqd", part_weights, value_rows, preferred_element_type=jnp.float32
        )
        outputs = (weighted / part_total).astype(jnp.bfloat16)
        halves.append(outputs.reshape(group_heads * capacity, BLK // 2, head_dim))
    outputs = jnp.concatenate(halves, axis=1)
    returned = lax.all_to_all(
        by_index(outputs, back_pick), "seq", split_axis=0, concat_axis=0, tiled=True
    )
    own_output = by_index(returned, own_pos).reshape(
        group_heads, group_count, own_blocks, BLK, head_dim
    )
    gathered = lax.all_to_all(own_output, "fsdp", split_axis=1, concat_axis=0, tiled=True)
    token_major = jnp.transpose(gathered[:, 0], (1, 2, 0, 3))
    return token_major.reshape(tok_rows, heads_all * head_dim)


def solution(mesh):
    placed = (P(("seq", "fsdp"), None), P(("seq", "fsdp"), None), P())
    return jax.shard_map(
        shards, mesh=mesh, in_specs=placed, out_specs=P(("seq", "fsdp"), None), check_vma=False
    )
```

```python
import math

import jax
import jax.numpy as jnp
from jax import lax
from jax.sharding import PartitionSpec as P

BLK = 128


masked_score = -1e30


def by_index(source_table, row_index):
    return source_table[jnp.clip(row_index, 0, source_table.shape[0] - 1)]


def softmax_group(key_rows, positions, alive_rows, score_scale):
    half = BLK // 2
    blocks = key_rows.shape[0] // BLK

    def by_half(rows):
        shaped = rows.reshape((blocks, 2, half) + rows.shape[1:])
        return jnp.swapaxes(shaped, 0, 1).reshape(rows.shape)

    query_rows = by_half(key_rows)
    query_positions = by_half(positions)
    query_alive = by_half(alive_rows)
    scores = jnp.dot(query_rows, key_rows.T, preferred_element_type=jnp.float32) * score_scale
    allowed = alive_rows[None, :] & (positions[None, :] <= query_positions[:, None])
    scores = jnp.where(allowed, scores, masked_score)
    row_peak = jnp.max(scores, axis=1, keepdims=True)
    weights = jnp.where(allowed, jnp.exp(scores - row_peak), 0.0)
    row_total = jnp.where(query_alive[:, None], jnp.sum(weights, axis=1, keepdims=True), 1.0)
    weights = weights.astype(jnp.bfloat16).reshape(2, blocks * half, key_rows.shape[0])
    row_total = row_total.reshape(2, blocks * half, 1)
    return weights[0], weights[1], row_total[0], row_total[1]


def shards(query_key, values, cluster_ids):
    seq_count = lax.axis_size("seq")
    group_count = lax.axis_size("fsdp")
    seq_index = lax.axis_index("seq")
    group_index = lax.axis_index("fsdp")
    heads_all = cluster_ids.shape[0]
    group_heads = heads_all // group_count
    head_dim = query_key.shape[1] // heads_all
    tok_rows = query_key.shape[0]
    shard_blocks = group_count * tok_rows // BLK
    all_blocks = cluster_ids.shape[1]
    item_count = group_heads * shard_blocks
    slot_count = max(1, item_count // seq_count)
    capacity = shard_blocks + min(shard_blocks // 4, seq_count - shard_blocks)
    group_rows = capacity * BLK
    send_rows = seq_count * slot_count
    score_scale = 1.0 / math.sqrt(head_dim)
    own_blocks = tok_rows // BLK

    keys_local = lax.all_to_all(query_key, "fsdp", split_axis=1, concat_axis=0, tiled=True)
    value_chunks = values.reshape(tok_rows, group_count, group_heads * head_dim)
    value_chunks, keys_local = lax.optimization_barrier((value_chunks, keys_local))
    by_shift = [lax.dynamic_index_in_dim(value_chunks, group_index, 1, keepdims=False)]
    for shift in range(1, group_count):
        outgoing = lax.dynamic_index_in_dim(
            value_chunks, (group_index + shift) % group_count, 1, keepdims=False
        )
        by_shift.append(
            lax.ppermute(
                outgoing,
                "fsdp",
                [(peer, (peer + shift) % group_count) for peer in range(group_count)],
            )
        )
    source_order = (group_index - jnp.arange(group_count, dtype=jnp.int32)) % group_count
    values_local = jnp.stack(by_shift)[source_order].reshape(
        group_count * tok_rows, group_heads * head_dim
    )

    def into_items(block_data):
        shaped = block_data.reshape(shard_blocks, BLK, group_heads, head_dim)
        return jnp.transpose(shaped, (2, 0, 1, 3)).reshape(item_count, BLK, head_dim)

    key_items = into_items(keys_local)
    value_items = into_items(values_local)
    group_ids = lax.dynamic_slice_in_dim(cluster_ids, group_index * group_heads, group_heads, 0)
    by_source = jnp.transpose(
        group_ids.reshape(group_heads, seq_count, shard_blocks), (1, 0, 2)
    ).reshape(seq_count, item_count)
    own_dest = lax.dynamic_index_in_dim(by_source, seq_index, 0, keepdims=False)
    item_ids = jnp.arange(item_count, dtype=jnp.int32)
    earlier = (own_dest[None, :] == own_dest[:, None]) & (item_ids[None, :] < item_ids[:, None])
    own_pos = own_dest * slot_count + jnp.sum(earlier.astype(jnp.int32), axis=1)
    row_ids = jnp.arange(send_rows, dtype=jnp.int32)
    slot_match = own_pos[None, :] == row_ids[:, None]
    send_pick = jnp.sum(jnp.where(slot_match, item_ids[None, :], 0), axis=1) + item_count * (
        1 - jnp.any(slot_match, axis=1).astype(jnp.int32)
    )
    received_mask = (by_source == seq_index).astype(jnp.int32)
    recv_pos = (
        jnp.arange(seq_count, dtype=jnp.int32)[:, None] * slot_count
        + jnp.cumsum(received_mask, axis=1)
        - received_mask
    )
    recv_by_head = jnp.transpose(
        recv_pos.reshape(seq_count, group_heads, shard_blocks), (1, 0, 2)
    ).reshape(group_heads * all_blocks)
    owned_mask = (group_ids == seq_index).astype(jnp.int32)
    ordinal = jnp.cumsum(owned_mask, axis=1) - owned_mask
    target = jnp.where(
        owned_mask > 0, jnp.arange(group_heads, dtype=jnp.int32)[:, None] * capacity + ordinal, -1
    ).reshape(group_heads * all_blocks)
    slot_ids = jnp.arange(group_heads * capacity, dtype=jnp.int32)
    matches = target[None, :] == slot_ids[:, None]
    present = jnp.any(matches, axis=1)
    source_row = jnp.sum(jnp.where(matches, recv_by_head[None, :], 0), axis=1) + send_rows * (
        1 - present.astype(jnp.int32)
    )
    block_ids = jnp.tile(jnp.arange(all_blocks, dtype=jnp.int32), group_heads)
    block_of = jnp.sum(jnp.where(matches, block_ids[None, :], 0), axis=1)
    arrived_k = lax.all_to_all(
        by_index(key_items, send_pick), "seq", split_axis=0, concat_axis=0, tiled=True
    )
    value_send = by_index(value_items, send_pick)
    arrived_k, value_send = lax.optimization_barrier((arrived_k, value_send))
    arrived_v = lax.all_to_all(value_send, "seq", split_axis=0, concat_axis=0, tiled=True)
    key_grouped = by_index(arrived_k, source_row)
    value_grouped = by_index(arrived_v, source_row)
    positions = (block_of[:, None] * BLK + jnp.arange(BLK, dtype=jnp.int32)[None, :]).reshape(
        group_heads, group_rows
    )
    alive_rows = jnp.repeat(present, BLK).reshape(group_heads, group_rows)

    def one_head(operands):
        key_rows, where_at, alive_here = operands
        return softmax_group(key_rows, where_at, alive_here, score_scale)

    weights_0, weights_1, totals_0, totals_1 = lax.map(
        one_head,
        (key_grouped.reshape(group_heads, group_rows, head_dim), positions, alive_rows),
    )
    value_rows = value_grouped.reshape(group_heads, group_rows, head_dim)
    back_match = source_row[None, :] == row_ids[:, None]
    back_pick = jnp.sum(
        jnp.where(back_match, slot_ids[None, :], 0), axis=1
    ) + group_heads * capacity * (1 - jnp.any(back_match, axis=1).astype(jnp.int32))
    halves = []
    for part_weights, part_total in ((weights_0, totals_0), (weights_1, totals_1)):
        weighted = jnp.einsum(
            "hqk,hkd->hqd", part_weights, value_rows, preferred_element_type=jnp.float32
        )
        outputs = (weighted / part_total).astype(jnp.bfloat16)
        halves.append(outputs.reshape(group_heads * capacity, BLK // 2, head_dim))
    outputs = jnp.concatenate(halves, axis=1)
    returned = lax.all_to_all(
        by_index(outputs, back_pick), "seq", split_axis=0, concat_axis=0, tiled=True
    )
    own_output = by_index(returned, own_pos).reshape(
        group_heads, group_count, own_blocks, BLK, head_dim
    )
    gathered = lax.all_to_all(
        jnp.swapaxes(own_output, 0, 1), "fsdp", split_axis=0, concat_axis=0, tiled=True
    )
    token_major = jnp.transpose(gathered, (2, 3, 0, 1, 4))
    return token_major.reshape(tok_rows, heads_all * head_dim)


def solution(mesh):
    placed = (P(("seq", "fsdp"), None), P(("seq", "fsdp"), None), P())
    return jax.shard_map(
        shards, mesh=mesh, in_specs=placed, out_specs=P(("seq", "fsdp"), None), check_vma=False
    )
```

```python
import math

import jax
import jax.numpy as jnp
from jax import lax
from jax.sharding import PartitionSpec as P

BLK = 128


masked_score = -1e30


def by_index(source_table, row_index):
    return source_table[jnp.clip(row_index, 0, source_table.shape[0] - 1)]


def fsdp_exchange(outgoing_by_dest, group_index, group_count):
    by_shift = [lax.dynamic_index_in_dim(outgoing_by_dest, group_index, 0, keepdims=False)]
    for shift in range(1, group_count):
        outgoing = lax.dynamic_index_in_dim(
            outgoing_by_dest, (group_index + shift) % group_count, 0, keepdims=False
        )
        by_shift.append(
            lax.ppermute(
                outgoing,
                "fsdp",
                [(peer, (peer + shift) % group_count) for peer in range(group_count)],
            )
        )
    source_order = (group_index - jnp.arange(group_count, dtype=jnp.int32)) % group_count
    return jnp.stack(by_shift)[source_order]


def softmax_group(key_rows, positions, alive_rows, score_scale):
    half = BLK // 2
    blocks = key_rows.shape[0] // BLK

    def by_half(rows):
        shaped = rows.reshape((blocks, 2, half) + rows.shape[1:])
        return jnp.swapaxes(shaped, 0, 1).reshape(rows.shape)

    query_rows = by_half(key_rows)
    query_positions = by_half(positions)
    query_alive = by_half(alive_rows)
    scores = jnp.dot(query_rows, key_rows.T, preferred_element_type=jnp.float32) * score_scale
    allowed = alive_rows[None, :] & (positions[None, :] <= query_positions[:, None])
    scores = jnp.where(allowed, scores, masked_score)
    row_peak = jnp.max(scores, axis=1, keepdims=True)
    weights = jnp.where(allowed, jnp.exp(scores - row_peak), 0.0)
    row_total = jnp.where(query_alive[:, None], jnp.sum(weights, axis=1, keepdims=True), 1.0)
    weights = weights.astype(jnp.bfloat16).reshape(2, blocks * half, key_rows.shape[0])
    row_total = row_total.reshape(2, blocks * half, 1)
    return weights[0], weights[1], row_total[0], row_total[1]


def shards(query_key, values, cluster_ids):
    seq_count = lax.axis_size("seq")
    group_count = lax.axis_size("fsdp")
    seq_index = lax.axis_index("seq")
    group_index = lax.axis_index("fsdp")
    heads_all = cluster_ids.shape[0]
    group_heads = heads_all // group_count
    head_dim = query_key.shape[1] // heads_all
    tok_rows = query_key.shape[0]
    shard_blocks = group_count * tok_rows // BLK
    all_blocks = cluster_ids.shape[1]
    item_count = group_heads * shard_blocks
    slot_count = max(1, item_count // seq_count)
    capacity = shard_blocks + min(shard_blocks // 4, seq_count - shard_blocks)
    group_rows = capacity * BLK
    send_rows = seq_count * slot_count
    score_scale = 1.0 / math.sqrt(head_dim)
    own_blocks = tok_rows // BLK

    keys_local = lax.all_to_all(query_key, "fsdp", split_axis=1, concat_axis=0, tiled=True)
    value_chunks = values.reshape(tok_rows, group_count, group_heads * head_dim)
    value_chunks, keys_local = lax.optimization_barrier((value_chunks, keys_local))
    by_shift = [lax.dynamic_index_in_dim(value_chunks, group_index, 1, keepdims=False)]
    for shift in range(1, group_count):
        outgoing = lax.dynamic_index_in_dim(
            value_chunks, (group_index + shift) % group_count, 1, keepdims=False
        )
        by_shift.append(
            lax.ppermute(
                outgoing,
                "fsdp",
                [(peer, (peer + shift) % group_count) for peer in range(group_count)],
            )
        )
    source_order = (group_index - jnp.arange(group_count, dtype=jnp.int32)) % group_count
    values_local = jnp.stack(by_shift)[source_order].reshape(
        group_count * tok_rows, group_heads * head_dim
    )

    def into_items(block_data):
        shaped = block_data.reshape(shard_blocks, BLK, group_heads, head_dim)
        return jnp.transpose(shaped, (2, 0, 1, 3)).reshape(item_count, BLK, head_dim)

    key_items = into_items(keys_local)
    value_items = into_items(values_local)
    group_ids = lax.dynamic_slice_in_dim(cluster_ids, group_index * group_heads, group_heads, 0)
    by_source = jnp.transpose(
        group_ids.reshape(group_heads, seq_count, shard_blocks), (1, 0, 2)
    ).reshape(seq_count, item_count)
    own_dest = lax.dynamic_index_in_dim(by_source, seq_index, 0, keepdims=False)
    item_ids = jnp.arange(item_count, dtype=jnp.int32)
    earlier = (own_dest[None, :] == own_dest[:, None]) & (item_ids[None, :] < item_ids[:, None])
    own_pos = own_dest * slot_count + jnp.sum(earlier.astype(jnp.int32), axis=1)
    row_ids = jnp.arange(send_rows, dtype=jnp.int32)
    slot_match = own_pos[None, :] == row_ids[:, None]
    send_pick = jnp.sum(jnp.where(slot_match, item_ids[None, :], 0), axis=1) + item_count * (
        1 - jnp.any(slot_match, axis=1).astype(jnp.int32)
    )
    received_mask = (by_source == seq_index).astype(jnp.int32)
    recv_pos = (
        jnp.arange(seq_count, dtype=jnp.int32)[:, None] * slot_count
        + jnp.cumsum(received_mask, axis=1)
        - received_mask
    )
    recv_by_head = jnp.transpose(
        recv_pos.reshape(seq_count, group_heads, shard_blocks), (1, 0, 2)
    ).reshape(group_heads * all_blocks)
    owned_mask = (group_ids == seq_index).astype(jnp.int32)
    ordinal = jnp.cumsum(owned_mask, axis=1) - owned_mask
    target = jnp.where(
        owned_mask > 0, jnp.arange(group_heads, dtype=jnp.int32)[:, None] * capacity + ordinal, -1
    ).reshape(group_heads * all_blocks)
    slot_ids = jnp.arange(group_heads * capacity, dtype=jnp.int32)
    matches = target[None, :] == slot_ids[:, None]
    present = jnp.any(matches, axis=1)
    source_row = jnp.sum(jnp.where(matches, recv_by_head[None, :], 0), axis=1) + send_rows * (
        1 - present.astype(jnp.int32)
    )
    block_ids = jnp.tile(jnp.arange(all_blocks, dtype=jnp.int32), group_heads)
    block_of = jnp.sum(jnp.where(matches, block_ids[None, :], 0), axis=1)
    arrived_k = lax.all_to_all(
        by_index(key_items, send_pick), "seq", split_axis=0, concat_axis=0, tiled=True
    )
    value_send = by_index(value_items, send_pick)
    arrived_k, value_send = lax.optimization_barrier((arrived_k, value_send))
    arrived_v = lax.all_to_all(value_send, "seq", split_axis=0, concat_axis=0, tiled=True)
    key_grouped = by_index(arrived_k, source_row)
    value_grouped = by_index(arrived_v, source_row)
    positions = (block_of[:, None] * BLK + jnp.arange(BLK, dtype=jnp.int32)[None, :]).reshape(
        group_heads, group_rows
    )
    alive_rows = jnp.repeat(present, BLK).reshape(group_heads, group_rows)

    def one_head(operands):
        key_rows, where_at, alive_here = operands
        return softmax_group(key_rows, where_at, alive_here, score_scale)

    weights_0, weights_1, totals_0, totals_1 = lax.map(
        one_head,
        (key_grouped.reshape(group_heads, group_rows, head_dim), positions, alive_rows),
    )
    value_rows = value_grouped.reshape(group_heads, group_rows, head_dim)
    back_match = source_row[None, :] == row_ids[:, None]
    back_pick = jnp.sum(
        jnp.where(back_match, slot_ids[None, :], 0), axis=1
    ) + group_heads * capacity * (1 - jnp.any(back_match, axis=1).astype(jnp.int32))
    halves = []
    for part_weights, part_total in ((weights_0, totals_0), (weights_1, totals_1)):
        weighted = jnp.einsum(
            "hqk,hkd->hqd", part_weights, value_rows, preferred_element_type=jnp.float32
        )
        outputs = (weighted / part_total).astype(jnp.bfloat16)
        halves.append(outputs.reshape(group_heads * capacity, BLK // 2, head_dim))
    outputs = jnp.concatenate(halves, axis=1)
    returned = lax.all_to_all(
        by_index(outputs, back_pick), "seq", split_axis=0, concat_axis=0, tiled=True
    )
    own_output = by_index(returned, own_pos).reshape(
        group_heads, group_count, own_blocks, BLK, head_dim
    )
    gathered = fsdp_exchange(jnp.swapaxes(own_output, 0, 1), group_index, group_count)
    token_major = jnp.transpose(gathered, (2, 3, 0, 1, 4))
    return token_major.reshape(tok_rows, heads_all * head_dim)


def solution(mesh):
    placed = (P(("seq", "fsdp"), None), P(("seq", "fsdp"), None), P())
    return jax.shard_map(
        shards, mesh=mesh, in_specs=placed, out_specs=P(("seq", "fsdp"), None), check_vma=False
    )
```

```python
import math

import jax
import jax.numpy as jnp
from jax import lax
from jax.sharding import PartitionSpec as P

BLK = 128


masked_score = -1e30


def by_index(source_table, row_index):
    return source_table[jnp.clip(row_index, 0, source_table.shape[0] - 1)]


def softmax_group(key_rows, positions, alive_rows, score_scale):
    scores = jnp.dot(key_rows, key_rows.T, preferred_element_type=jnp.float32) * score_scale
    allowed = alive_rows[None, :] & (positions[None, :] <= positions[:, None])
    scores = jnp.where(allowed, scores, masked_score)
    row_peak = jnp.max(scores, axis=1, keepdims=True)
    weights = jnp.where(allowed, jnp.exp(scores - row_peak), 0.0)
    row_total = jnp.where(alive_rows[:, None], jnp.sum(weights, axis=1, keepdims=True), 1.0)
    return weights.astype(jnp.bfloat16), row_total


def shards(query_key, values, cluster_ids):
    seq_count = lax.axis_size("seq")
    group_count = lax.axis_size("fsdp")
    seq_index = lax.axis_index("seq")
    group_index = lax.axis_index("fsdp")
    heads_all = cluster_ids.shape[0]
    group_heads = heads_all // group_count
    head_dim = query_key.shape[1] // heads_all
    tok_rows = query_key.shape[0]
    shard_blocks = group_count * tok_rows // BLK
    all_blocks = cluster_ids.shape[1]
    item_count = group_heads * shard_blocks
    slot_count = max(1, item_count // seq_count)
    capacity = shard_blocks + min(shard_blocks // 4, seq_count - shard_blocks)
    group_rows = capacity * BLK
    send_rows = seq_count * slot_count
    score_scale = 1.0 / math.sqrt(head_dim)
    own_blocks = tok_rows // BLK

    keys_local = lax.all_to_all(query_key, "fsdp", split_axis=1, concat_axis=0, tiled=True)
    value_chunks = values.reshape(tok_rows, group_count, group_heads * head_dim)
    value_chunks, keys_local = lax.optimization_barrier((value_chunks, keys_local))
    by_shift = [lax.dynamic_index_in_dim(value_chunks, group_index, 1, keepdims=False)]
    for shift in range(1, group_count):
        outgoing = lax.dynamic_index_in_dim(
            value_chunks, (group_index + shift) % group_count, 1, keepdims=False
        )
        by_shift.append(
            lax.ppermute(
                outgoing,
                "fsdp",
                [(peer, (peer + shift) % group_count) for peer in range(group_count)],
            )
        )
    source_order = (group_index - jnp.arange(group_count, dtype=jnp.int32)) % group_count
    values_local = jnp.stack(by_shift)[source_order].reshape(
        group_count * tok_rows, group_heads * head_dim
    )

    def into_items(block_data):
        shaped = block_data.reshape(shard_blocks, BLK, group_heads, head_dim)
        return jnp.transpose(shaped, (2, 0, 1, 3)).reshape(item_count, BLK, head_dim)

    key_items = into_items(keys_local)
    value_items = into_items(values_local)
    group_ids = lax.dynamic_slice_in_dim(cluster_ids, group_index * group_heads, group_heads, 0)
    by_source = jnp.transpose(
        group_ids.reshape(group_heads, seq_count, shard_blocks), (1, 0, 2)
    ).reshape(seq_count, item_count)
    own_dest = lax.dynamic_index_in_dim(by_source, seq_index, 0, keepdims=False)
    item_ids = jnp.arange(item_count, dtype=jnp.int32)
    earlier = (own_dest[None, :] == own_dest[:, None]) & (item_ids[None, :] < item_ids[:, None])
    own_pos = own_dest * slot_count + jnp.sum(earlier.astype(jnp.int32), axis=1)
    row_ids = jnp.arange(send_rows, dtype=jnp.int32)
    slot_match = own_pos[None, :] == row_ids[:, None]
    send_pick = jnp.sum(jnp.where(slot_match, item_ids[None, :], 0), axis=1) + item_count * (
        1 - jnp.any(slot_match, axis=1).astype(jnp.int32)
    )
    received_mask = (by_source == seq_index).astype(jnp.int32)
    recv_pos = (
        jnp.arange(seq_count, dtype=jnp.int32)[:, None] * slot_count
        + jnp.cumsum(received_mask, axis=1)
        - received_mask
    )
    recv_by_head = jnp.transpose(
        recv_pos.reshape(seq_count, group_heads, shard_blocks), (1, 0, 2)
    ).reshape(group_heads * all_blocks)
    owned_mask = (group_ids == seq_index).astype(jnp.int32)
    ordinal = jnp.cumsum(owned_mask, axis=1) - owned_mask
    target = jnp.where(
        owned_mask > 0, jnp.arange(group_heads, dtype=jnp.int32)[:, None] * capacity + ordinal, -1
    ).reshape(group_heads * all_blocks)
    slot_ids = jnp.arange(group_heads * capacity, dtype=jnp.int32)
    matches = target[None, :] == slot_ids[:, None]
    present = jnp.any(matches, axis=1)
    source_row = jnp.sum(jnp.where(matches, recv_by_head[None, :], 0), axis=1) + send_rows * (
        1 - present.astype(jnp.int32)
    )
    block_ids = jnp.tile(jnp.arange(all_blocks, dtype=jnp.int32), group_heads)
    block_of = jnp.sum(jnp.where(matches, block_ids[None, :], 0), axis=1)
    arrived_k = lax.all_to_all(
        by_index(key_items, send_pick), "seq", split_axis=0, concat_axis=0, tiled=True
    )
    value_send = by_index(value_items, send_pick)
    arrived_k, value_send = lax.optimization_barrier((arrived_k, value_send))
    arrived_v = lax.all_to_all(value_send, "seq", split_axis=0, concat_axis=0, tiled=True)
    key_grouped = by_index(arrived_k, source_row)
    value_grouped = by_index(arrived_v, source_row)
    positions = (block_of[:, None] * BLK + jnp.arange(BLK, dtype=jnp.int32)[None, :]).reshape(
        group_heads, group_rows
    )
    alive_rows = jnp.repeat(present, BLK).reshape(group_heads, group_rows)

    def one_head(operands):
        key_rows, where_at, alive_here = operands
        return softmax_group(key_rows, where_at, alive_here, score_scale)

    weights, totals = lax.map(
        one_head,
        (key_grouped.reshape(group_heads, group_rows, head_dim), positions, alive_rows),
    )
    value_rows = value_grouped.reshape(group_heads, group_rows, head_dim)
    back_match = source_row[None, :] == row_ids[:, None]
    back_pick = jnp.sum(
        jnp.where(back_match, slot_ids[None, :], 0), axis=1
    ) + group_heads * capacity * (1 - jnp.any(back_match, axis=1).astype(jnp.int32))
    weighted = jnp.einsum("hqk,hkd->hqd", weights, value_rows, preferred_element_type=jnp.float32)
    outputs = (weighted / totals).astype(jnp.bfloat16).reshape(group_heads * capacity, BLK, head_dim)
    returned = lax.all_to_all(
        by_index(outputs, back_pick), "seq", split_axis=0, concat_axis=0, tiled=True
    )
    own_output = by_index(returned, own_pos).reshape(
        group_heads, group_count, own_blocks, BLK, head_dim
    )
    gathered = lax.all_to_all(
        jnp.swapaxes(own_output, 0, 1), "fsdp", split_axis=0, concat_axis=0, tiled=True
    )
    token_major = jnp.transpose(gathered, (2, 3, 0, 1, 4))
    return token_major.reshape(tok_rows, heads_all * head_dim)


def solution(mesh):
    placed = (P(("seq", "fsdp"), None), P(("seq", "fsdp"), None), P())
    return jax.shard_map(
        shards, mesh=mesh, in_specs=placed, out_specs=P(("seq", "fsdp"), None), check_vma=False
    )
```

```python
import math

import jax
import jax.numpy as jnp
from jax import lax
from jax.sharding import PartitionSpec as P

BLK = 128


masked_score = -1e30


def by_index(source_table, row_index):
    return source_table[jnp.clip(row_index, 0, source_table.shape[0] - 1)]


def softmax_group(key_rows, positions, alive_rows, score_scale):
    scores = jnp.dot(key_rows, key_rows.T, preferred_element_type=jnp.float32) * score_scale
    allowed = alive_rows[None, :] & (positions[None, :] <= positions[:, None])
    scores = jnp.where(allowed, scores, masked_score)
    row_peak = jnp.max(scores, axis=1, keepdims=True)
    weights = jnp.where(allowed, jnp.exp(scores - row_peak), 0.0)
    row_total = jnp.where(alive_rows[:, None], jnp.sum(weights, axis=1, keepdims=True), 1.0)
    return weights.astype(jnp.bfloat16), row_total


def shards(query_key, values, cluster_ids):
    seq_count = lax.axis_size("seq")
    group_count = lax.axis_size("fsdp")
    seq_index = lax.axis_index("seq")
    group_index = lax.axis_index("fsdp")
    heads_all = cluster_ids.shape[0]
    group_heads = heads_all // group_count
    head_dim = query_key.shape[1] // heads_all
    tok_rows = query_key.shape[0]
    shard_blocks = group_count * tok_rows // BLK
    all_blocks = cluster_ids.shape[1]
    item_count = group_heads * shard_blocks
    slot_count = max(1, item_count // seq_count)
    capacity = shard_blocks + min(shard_blocks // 4, seq_count - shard_blocks)
    group_rows = capacity * BLK
    send_rows = seq_count * slot_count
    score_scale = 1.0 / math.sqrt(head_dim)
    own_blocks = tok_rows // BLK

    keys_local = lax.all_to_all(query_key, "fsdp", split_axis=1, concat_axis=0, tiled=True)
    value_chunks = values.reshape(tok_rows, group_count, group_heads * head_dim)
    value_chunks, keys_local = lax.optimization_barrier((value_chunks, keys_local))
    by_shift = [lax.dynamic_index_in_dim(value_chunks, group_index, 1, keepdims=False)]
    for shift in range(1, group_count):
        outgoing = lax.dynamic_index_in_dim(
            value_chunks, (group_index + shift) % group_count, 1, keepdims=False
        )
        by_shift.append(
            lax.ppermute(
                outgoing,
                "fsdp",
                [(peer, (peer + shift) % group_count) for peer in range(group_count)],
            )
        )
    source_order = (group_index - jnp.arange(group_count, dtype=jnp.int32)) % group_count
    values_local = jnp.stack(by_shift)[source_order].reshape(
        group_count * tok_rows, group_heads * head_dim
    )

    def into_items(block_data):
        shaped = block_data.reshape(shard_blocks, BLK, group_heads, head_dim)
        return jnp.transpose(shaped, (2, 0, 1, 3)).reshape(item_count, BLK, head_dim)

    key_items = into_items(keys_local)
    value_items = into_items(values_local)
    group_ids = lax.dynamic_slice_in_dim(cluster_ids, group_index * group_heads, group_heads, 0)
    by_source = jnp.transpose(
        group_ids.reshape(group_heads, seq_count, shard_blocks), (1, 0, 2)
    ).reshape(seq_count, item_count)
    own_dest = lax.dynamic_index_in_dim(by_source, seq_index, 0, keepdims=False)
    item_ids = jnp.arange(item_count, dtype=jnp.int32)
    earlier = (own_dest[None, :] == own_dest[:, None]) & (item_ids[None, :] < item_ids[:, None])
    own_pos = own_dest * slot_count + jnp.sum(earlier.astype(jnp.int32), axis=1)
    row_ids = jnp.arange(send_rows, dtype=jnp.int32)
    slot_match = own_pos[None, :] == row_ids[:, None]
    send_pick = jnp.sum(jnp.where(slot_match, item_ids[None, :], 0), axis=1) + item_count * (
        1 - jnp.any(slot_match, axis=1).astype(jnp.int32)
    )
    key_send, group_ids = lax.optimization_barrier((by_index(key_items, send_pick), group_ids))
    arrived_k = lax.all_to_all(key_send, "seq", split_axis=0, concat_axis=0, tiled=True)
    value_send = by_index(value_items, send_pick)
    arrived_k, value_send = lax.optimization_barrier((arrived_k, value_send))
    arrived_v = lax.all_to_all(value_send, "seq", split_axis=0, concat_axis=0, tiled=True)
    by_source = jnp.transpose(
        group_ids.reshape(group_heads, seq_count, shard_blocks), (1, 0, 2)
    ).reshape(seq_count, item_count)
    received_mask = (by_source == seq_index).astype(jnp.int32)
    recv_pos = (
        jnp.arange(seq_count, dtype=jnp.int32)[:, None] * slot_count
        + jnp.cumsum(received_mask, axis=1)
        - received_mask
    )
    recv_by_head = jnp.transpose(
        recv_pos.reshape(seq_count, group_heads, shard_blocks), (1, 0, 2)
    ).reshape(group_heads * all_blocks)
    owned_mask = (group_ids == seq_index).astype(jnp.int32)
    ordinal = jnp.cumsum(owned_mask, axis=1) - owned_mask
    target = jnp.where(
        owned_mask > 0, jnp.arange(group_heads, dtype=jnp.int32)[:, None] * capacity + ordinal, -1
    ).reshape(group_heads * all_blocks)
    slot_ids = jnp.arange(group_heads * capacity, dtype=jnp.int32)
    matches = target[None, :] == slot_ids[:, None]
    present = jnp.any(matches, axis=1)
    source_row = jnp.sum(jnp.where(matches, recv_by_head[None, :], 0), axis=1) + send_rows * (
        1 - present.astype(jnp.int32)
    )
    block_ids = jnp.tile(jnp.arange(all_blocks, dtype=jnp.int32), group_heads)
    block_of = jnp.sum(jnp.where(matches, block_ids[None, :], 0), axis=1)
    key_grouped = by_index(arrived_k, source_row)
    value_grouped = by_index(arrived_v, source_row)
    positions = (block_of[:, None] * BLK + jnp.arange(BLK, dtype=jnp.int32)[None, :]).reshape(
        group_heads, group_rows
    )
    alive_rows = jnp.repeat(present, BLK).reshape(group_heads, group_rows)

    def one_head(operands):
        key_rows, where_at, alive_here = operands
        return softmax_group(key_rows, where_at, alive_here, score_scale)

    weights, totals = lax.map(
        one_head,
        (key_grouped.reshape(group_heads, group_rows, head_dim), positions, alive_rows),
    )
    value_rows = value_grouped.reshape(group_heads, group_rows, head_dim)
    back_match = source_row[None, :] == row_ids[:, None]
    back_pick = jnp.sum(
        jnp.where(back_match, slot_ids[None, :], 0), axis=1
    ) + group_heads * capacity * (1 - jnp.any(back_match, axis=1).astype(jnp.int32))
    weighted = jnp.einsum("hqk,hkd->hqd", weights, value_rows, preferred_element_type=jnp.float32)
    outputs = (weighted / totals).astype(jnp.bfloat16).reshape(group_heads * capacity, BLK, head_dim)
    returned = lax.all_to_all(
        by_index(outputs, back_pick), "seq", split_axis=0, concat_axis=0, tiled=True
    )
    own_output = by_index(returned, own_pos).reshape(
        group_heads, group_count, own_blocks, BLK, head_dim
    )
    gathered = lax.all_to_all(
        jnp.swapaxes(own_output, 0, 1), "fsdp", split_axis=0, concat_axis=0, tiled=True
    )
    token_major = jnp.transpose(gathered, (2, 3, 0, 1, 4))
    return token_major.reshape(tok_rows, heads_all * head_dim)


def solution(mesh):
    placed = (P(("seq", "fsdp"), None), P(("seq", "fsdp"), None), P())
    return jax.shard_map(
        shards, mesh=mesh, in_specs=placed, out_specs=P(("seq", "fsdp"), None), check_vma=False
    )
```

```python
import math

import jax
import jax.numpy as jnp
from jax import lax
from jax.sharding import PartitionSpec as P

BLK = 128


masked_score = -1e30


def by_index(source_table, row_index):
    return source_table[jnp.clip(row_index, 0, source_table.shape[0] - 1)]


def softmax_group(key_rows, positions, alive_rows, score_scale):
    scores = jnp.dot(key_rows, key_rows.T, preferred_element_type=jnp.float32) * score_scale
    allowed = alive_rows[None, :] & (positions[None, :] <= positions[:, None])
    scores = jnp.where(allowed, scores, masked_score)
    row_peak = jnp.max(scores, axis=1, keepdims=True)
    weights = jnp.where(allowed, jnp.exp(scores - row_peak), 0.0)
    row_total = jnp.where(alive_rows[:, None], jnp.sum(weights, axis=1, keepdims=True), 1.0)
    return weights.astype(jnp.bfloat16), row_total


def shards(query_key, values, cluster_ids):
    seq_count = lax.axis_size("seq")
    group_count = lax.axis_size("fsdp")
    seq_index = lax.axis_index("seq")
    group_index = lax.axis_index("fsdp")
    heads_all = cluster_ids.shape[0]
    group_heads = heads_all // group_count
    head_dim = query_key.shape[1] // heads_all
    tok_rows = query_key.shape[0]
    shard_blocks = group_count * tok_rows // BLK
    all_blocks = cluster_ids.shape[1]
    item_count = group_heads * shard_blocks
    slot_count = max(1, item_count // seq_count)
    capacity = shard_blocks + min(shard_blocks // 4, seq_count - shard_blocks)
    group_rows = capacity * BLK
    send_rows = seq_count * slot_count
    score_scale = 1.0 / math.sqrt(head_dim)
    own_blocks = tok_rows // BLK

    keys_local = lax.all_to_all(query_key, "fsdp", split_axis=1, concat_axis=0, tiled=True)
    value_chunks = values.reshape(tok_rows, group_count, group_heads * head_dim)
    value_chunks, keys_local = lax.optimization_barrier((value_chunks, keys_local))
    by_shift = [lax.dynamic_index_in_dim(value_chunks, group_index, 1, keepdims=False)]
    for shift in range(1, group_count):
        outgoing = lax.dynamic_index_in_dim(
            value_chunks, (group_index + shift) % group_count, 1, keepdims=False
        )
        by_shift.append(
            lax.ppermute(
                outgoing,
                "fsdp",
                [(peer, (peer + shift) % group_count) for peer in range(group_count)],
            )
        )
    source_order = (group_index - jnp.arange(group_count, dtype=jnp.int32)) % group_count
    values_local = jnp.stack(by_shift)[source_order].reshape(
        group_count * tok_rows, group_heads * head_dim
    )

    def into_items(block_data):
        shaped = block_data.reshape(shard_blocks, BLK, group_heads, head_dim)
        return jnp.transpose(shaped, (2, 0, 1, 3)).reshape(item_count, BLK, head_dim)

    key_items = into_items(keys_local)
    value_items = into_items(values_local)
    group_ids = lax.dynamic_slice_in_dim(cluster_ids, group_index * group_heads, group_heads, 0)
    by_source = jnp.transpose(
        group_ids.reshape(group_heads, seq_count, shard_blocks), (1, 0, 2)
    ).reshape(seq_count, item_count)
    own_dest = lax.dynamic_index_in_dim(by_source, seq_index, 0, keepdims=False)
    item_ids = jnp.arange(item_count, dtype=jnp.int32)
    earlier = (own_dest[None, :] == own_dest[:, None]) & (item_ids[None, :] < item_ids[:, None])
    own_pos = own_dest * slot_count + jnp.sum(earlier.astype(jnp.int32), axis=1)
    row_ids = jnp.arange(send_rows, dtype=jnp.int32)
    slot_match = own_pos[None, :] == row_ids[:, None]
    send_pick = jnp.sum(jnp.where(slot_match, item_ids[None, :], 0), axis=1) + item_count * (
        1 - jnp.any(slot_match, axis=1).astype(jnp.int32)
    )
    key_send, group_ids = lax.optimization_barrier((by_index(key_items, send_pick), group_ids))
    arrived_k = lax.all_to_all(key_send, "seq", split_axis=0, concat_axis=0, tiled=True)
    value_send = by_index(value_items, send_pick)
    arrived_k, value_send = lax.optimization_barrier((arrived_k, value_send))
    arrived_v = lax.all_to_all(value_send, "seq", split_axis=0, concat_axis=0, tiled=True)
    by_source = jnp.transpose(
        group_ids.reshape(group_heads, seq_count, shard_blocks), (1, 0, 2)
    ).reshape(seq_count, item_count)
    received_mask = (by_source == seq_index).astype(jnp.int32)
    recv_pos = (
        jnp.arange(seq_count, dtype=jnp.int32)[:, None] * slot_count
        + jnp.cumsum(received_mask, axis=1)
        - received_mask
    )
    recv_by_head = jnp.transpose(
        recv_pos.reshape(seq_count, group_heads, shard_blocks), (1, 0, 2)
    ).reshape(group_heads * all_blocks)
    owned_mask = (group_ids == seq_index).astype(jnp.int32)
    ordinal = jnp.cumsum(owned_mask, axis=1) - owned_mask
    target = jnp.where(
        owned_mask > 0, jnp.arange(group_heads, dtype=jnp.int32)[:, None] * capacity + ordinal, -1
    ).reshape(group_heads * all_blocks)
    slot_ids = jnp.arange(group_heads * capacity, dtype=jnp.int32)
    matches = target[None, :] == slot_ids[:, None]
    present = jnp.any(matches, axis=1)
    source_row = jnp.sum(jnp.where(matches, recv_by_head[None, :], 0), axis=1) + send_rows * (
        1 - present.astype(jnp.int32)
    )
    block_ids = jnp.tile(jnp.arange(all_blocks, dtype=jnp.int32), group_heads)
    block_of = jnp.sum(jnp.where(matches, block_ids[None, :], 0), axis=1)
    key_grouped = by_index(arrived_k, source_row)
    value_grouped = by_index(arrived_v, source_row)
    positions = (block_of[:, None] * BLK + jnp.arange(BLK, dtype=jnp.int32)[None, :]).reshape(
        group_heads, group_rows
    )
    alive_rows = jnp.repeat(present, BLK).reshape(group_heads, group_rows)

    def one_head(operands):
        key_rows, where_at, alive_here = operands
        return softmax_group(key_rows, where_at, alive_here, score_scale)

    weights, totals = lax.map(
        one_head,
        (key_grouped.reshape(group_heads, group_rows, head_dim), positions, alive_rows),
    )
    value_rows = value_grouped.reshape(group_heads, group_rows, head_dim)
    back_match = source_row[None, :] == row_ids[:, None]
    back_pick = jnp.sum(
        jnp.where(back_match, slot_ids[None, :], 0), axis=1
    ) + group_heads * capacity * (1 - jnp.any(back_match, axis=1).astype(jnp.int32))
    weighted = jnp.einsum("hqk,hkd->hqd", weights, value_rows, preferred_element_type=jnp.float32)
    outputs = (weighted / totals).astype(jnp.bfloat16).reshape(group_heads * capacity, BLK, head_dim)
    returned = lax.all_to_all(
        by_index(outputs, back_pick), "seq", split_axis=0, concat_axis=0, tiled=True
    )
    own_output = by_index(returned, own_pos)
    token_major = jnp.transpose(
        own_output.reshape(group_heads, shard_blocks, BLK, head_dim), (1, 2, 0, 3)
    ).reshape(shard_blocks * BLK, group_heads * head_dim)
    return lax.all_to_all(token_major, "fsdp", split_axis=0, concat_axis=1, tiled=True)


def solution(mesh):
    placed = (P(("seq", "fsdp"), None), P(("seq", "fsdp"), None), P())
    return jax.shard_map(
        shards, mesh=mesh, in_specs=placed, out_specs=P(("seq", "fsdp"), None), check_vma=False
    )
```
